128 devices in a mesh: month: 4 (over x), grid: 32 (over y, z, core).
Axes of the slice: x: 4, y: 4, z: 4, core: 2. Of those that a mesh axis runs over, the one named last changes fastest.
Arguments:
- tracers: float32 [64, 32768], P(None, 'grid'), may hold values from 0.25 to 7
- targets: float32 [64], replicated, may hold values from 0.5 to 2
- retain: float32 [8, 32768], P('month', 'grid'), may hold values from 0.5 to 0.95
- blocks: float32 [8, 256, 8, 128, 128], P('month', 'grid'), may hold values from 3.90625e-07 to 0.00390625
- cols: int32 [8, 256, 8], P('month', 'grid'), may hold values from 0 to 255, as said below
Outputs:
- spun_up: float32 [64, 32768], P('month', 'grid')
The draws below stay inside these ranges and needn't reach their ends.
Inputs may be any that keep to these rules, and one draw needn't show every extreme that they name: cols[m, i, 0] = i; for 1 <= k < 6, cols[m, i, k] names a block on the same grid device as block i (block b lies on device b // 8); the last 2 entries name blocks on other devices, and of the 16 such entries of one device's block rows in one month at most 1 lie on any single device, exactly 1 on some.
All inputs are finite; a program needn't handle non-finite values.
Results may differ from the reference program's by a relative error of at most 0.0001.
Values sent between devices are 32-bit elements; how exact they have to be, the bound alone decides.
No kernel may reach another device: no remote copies, remote signals or barrier semaphores. Data moves between devices by JAX's collectives and lax.ppermute only.
A program may use at most 64 MiB of HBM per device.

```python
import math
import jax
import jax.numpy as jnp
from jax import lax

BS = 128
NB_DEV = 8
K = 8
KF = 2
MONTHS = 8
TRACERS = 64
NBLK = 256
NPTS = 32768
CAP = 1
N_GRID = 32


def draw_tracers(key, part):
    ramp_pos = jnp.arange(NPTS, dtype=jnp.float32) / NPTS
    base = jax.random.uniform(key, (TRACERS, NPTS), jnp.float32, 0.5, 1.5)
    ramp = 1.0 + 2.0 * ramp_pos
    return (base * ramp[None, :]).astype(jnp.float32)


def device_cols(dev_key, owner):
    keys = jax.random.split(dev_key, 5)
    far_count = NB_DEV * KF
    slots_all = CAP * (N_GRID - 1)
    diag_col = owner * NB_DEV + jnp.arange(NB_DEV, dtype=jnp.int32)
    near = jax.random.randint(keys[0], (NB_DEV, K - KF - 1), 0, NB_DEV).astype(jnp.int32) + owner * NB_DEV
    rest = jax.random.permutation(keys[1], slots_all - CAP).astype(jnp.int32) + CAP
    values = jnp.concatenate([jnp.arange(CAP, dtype=jnp.int32), rest[:far_count - CAP]])
    values = values[jax.random.permutation(keys[2], far_count)]
    peer_map = jax.random.permutation(keys[3], N_GRID - 1).astype(jnp.int32)
    peer = (owner + 1 + peer_map[values // CAP]) % N_GRID
    inner = jax.random.randint(keys[4], (far_count,), 0, NB_DEV).astype(jnp.int32)
    far = (peer * NB_DEV + inner).reshape(NB_DEV, KF)
    return jnp.concatenate([diag_col[:, None], near, far], axis=1)


def draw_cols(key, part):
    own_key = jax.random.fold_in(key, 7)
    keys = jax.random.split(own_key, MONTHS * N_GRID)
    owners = (jnp.arange(MONTHS * N_GRID, dtype=jnp.int32) % N_GRID).astype(jnp.int32)
    table = jax.vmap(device_cols)(keys, owners)
    return table.reshape(MONTHS, NBLK, K).astype(jnp.int32)


def level_of(key, shape, shards, low, top_value):
    gain = 1.0
    for dim, blocks in shards:
        heights = jax.random.uniform(jax.random.fold_in(jax.random.fold_in(key, 6), dim), (blocks,), jnp.float32, low / len(shards), top_value / len(shards))
        gain = gain * jnp.repeat(jnp.exp(heights), shape[dim] // blocks).reshape((-1,) + (1,) * (len(shape) - 1 - dim))
    return gain


def setup_inputs(seed: int = 0) -> dict:
    splits = jax.random.split(jax.random.key(seed), 6)
    tracers = draw_tracers(jax.random.fold_in(splits[5], 71), 0)
    targets = jnp.clip(jnp.exp(jax.random.uniform(splits[1], (TRACERS,), jnp.float32, math.log(0.5), math.log(2.0))), 0.5, 2.0)
    retain = jnp.clip(jnp.exp(math.log(0.95) - 0.64185387 * jax.random.uniform(splits[2], (MONTHS, NPTS), jnp.float32) ** level_of(splits[2], (MONTHS, NPTS), ((0, 4), (1, 32)), -0.2, 0.2)), 0.5, 0.95)
    blocks = jnp.clip(jnp.exp(math.log(0.00390625) - 9.2103404 * jax.random.uniform(splits[3], (MONTHS, NBLK, K, BS, BS), jnp.float32) ** level_of(splits[3], (MONTHS, NBLK, K, BS, BS), ((0, 4), (1, 32)), -0.2, 0.2)), 3.906249901319825e-07, 0.00390625)
    cols = draw_cols(jax.random.fold_in(splits[5], 71), 0)
    return dict(tracers=tracers, targets=targets, retain=retain, blocks=blocks, cols=cols)


def reference(tracers, targets, retain, blocks, cols):
    state = tracers
    for month_idx in range(MONTHS):
        view = state.reshape(TRACERS, NBLK, BS)
        picked = view[:, cols[month_idx]]
        mixed = jnp.einsum("tbkc,bkrc->tbr", picked, blocks[month_idx], precision=lax.Precision.HIGHEST, preferred_element_type=jnp.float32)
        state = retain[month_idx][None, :] * state + mixed.reshape(TRACERS, NPTS)
    inventory = jnp.sum(state, axis=1)
    return state * (targets * NPTS / inventory)[:, None]
```

```python
import jax
import jax.numpy as jnp
from jax import lax
from jax.sharding import PartitionSpec as P

NBATCH = 2
PRECISION = lax.Precision.HIGHEST


def exchange(x, axis):
    return lax.all_to_all(x, axis, 0, 0, tiled=True)


def local(tracers, targets, retain, blocks, cols):
    sections = lax.axis_size("month")
    devices = lax.axis_size("grid")
    section = lax.axis_index("month")
    me = lax.axis_index("grid")
    months_here = blocks.shape[0]
    blk_count = blocks.shape[1]
    nk = blocks.shape[2]
    blk_size = blocks.shape[3]
    rows_here = blk_count * blk_size
    points = rows_here * devices
    tracer_count = tracers.shape[0]
    batch = tracer_count // NBATCH
    own = tracer_count // sections

    src_dev = cols // blk_count
    src_blk = cols % blk_count
    is_far = src_dev != me
    req = jnp.full((months_here, devices), -1, jnp.int32)
    for j in range(months_here):
        d = jnp.where(is_far[j], src_dev[j], devices).reshape(-1)
        req = req.at[j, d].set(src_blk[j].reshape(-1), mode="drop")
    want = exchange(req.T, "grid")
    send_idx = jnp.maximum(want, 0)
    pick = jnp.where(is_far, blk_count + src_dev, src_blk)

    def apply_month(state, j):
        sb = state.reshape(batch, blk_count, blk_size)
        out = jnp.take(sb, send_idx[:, j], axis=1)
        got = exchange(out.transpose(1, 0, 2), "grid").transpose(1, 0, 2)
        ext = jnp.concatenate([sb, got], axis=1)
        picked = jnp.take(ext, pick[j].reshape(-1), axis=1).reshape(batch, blk_count, nk, blk_size)
        mixed = jnp.einsum(
            "tbkc,bkrc->tbr",
            picked,
            blocks[j],
            precision=PRECISION,
            preferred_element_type=jnp.float32,
        )
        return retain[j][None, :] * state + mixed.reshape(batch, rows_here)

    held = jnp.zeros((batch, rows_here), jnp.float32)
    done = []
    steps = NBATCH + sections - 1
    for step in range(steps):
        if step < NBATCH:
            held = jnp.where(section == 0, tracers[step * batch : (step + 1) * batch], held)
        for j in range(months_here):
            held = apply_month(held, j)
        if step >= sections - 1:
            done.append(held)
        if step < steps - 1:
            held = lax.ppermute(held, "month", [(i, (i + 1) % sections) for i in range(sections)])
    final = jnp.concatenate(done, axis=0)
    part = jnp.sum(final, axis=1)
    inventory = jnp.sum(exchange(jnp.broadcast_to(part[None], (devices, tracer_count)), "grid"), axis=0)
    scaled = final * (targets * points / inventory)[:, None]
    result = scaled[(sections - 1) * own :]
    last = sections - 1
    for dst in range(sections - 1):
        moved = lax.ppermute(scaled[dst * own : (dst + 1) * own], "month", [(last, dst)])
        result = jnp.where(section == dst, moved, result)
    return result


def solution(mesh):
    return jax.shard_map(
        local,
        mesh=mesh,
        in_specs=(
            P(None, "grid"),
            P(),
            P("month", "grid"),
            P("month", "grid", None, None, None),
            P("month", "grid", None),
        ),
        out_specs=P("month", "grid"),
        check_vma=False,
    )
```

```python
import jax
import jax.numpy as jnp
from jax import lax
from jax.sharding import PartitionSpec as P

NBATCH = 2
PRECISION = lax.Precision.HIGH
FAR = 2


def exchange(x, axis):
    return lax.all_to_all(x, axis, 0, 0, tiled=True)


def local(tracers, targets, retain, blocks, cols):
    sections = lax.axis_size("month")
    devices = lax.axis_size("grid")
    section = lax.axis_index("month")
    me = lax.axis_index("grid")
    months_here = blocks.shape[0]
    blk_count = blocks.shape[1]
    nk = blocks.shape[2]
    blk_size = blocks.shape[3]
    rows_here = blk_count * blk_size
    points = rows_here * devices
    tracer_count = tracers.shape[0]
    batch = tracer_count // NBATCH
    own = tracer_count // sections

    src_dev = cols // blk_count
    src_blk = cols % blk_count
    near = nk - FAR
    far_dev = src_dev[:, :, near:].reshape(months_here, -1)
    far_blk = src_blk[:, :, near:].reshape(months_here, -1)
    hit = far_dev[:, None, :] == jnp.arange(devices, dtype=jnp.int32)[None, :, None]
    req = jnp.sum(jnp.where(hit, far_blk[:, None, :] + 1, 0), axis=2) - 1

    last_m = months_here - 1
    colsum = jnp.sum(blocks[last_m], axis=2)
    to_blk = src_blk[last_m, :, :near][:, :, None] == jnp.arange(blk_count, dtype=jnp.int32)[None, None, :]
    c_loc = jnp.sum(jnp.where(to_blk[:, :, :, None], colsum[:, :near, None, :], 0.0), axis=(0, 1))
    far_cs = colsum[:, near:].reshape(-1, blk_size)
    cs_send = jnp.sum(jnp.where(hit[last_m][:, :, None], far_cs[None], 0.0), axis=1)
    sent = jnp.concatenate([cs_send, req.T.astype(jnp.float32)], axis=1)
    recv = exchange(sent, "grid")
    want = jnp.round(recv[:, blk_size:]).astype(jnp.int32)
    send_idx = jnp.maximum(want, 0)
    from_e = want[:, last_m][:, None] == jnp.arange(blk_count, dtype=jnp.int32)[None, :]
    c_far = jnp.sum(jnp.where(from_e[:, :, None], recv[:, None, :blk_size], 0.0), axis=0)
    c_all = (retain[last_m].reshape(blk_count, blk_size) + c_loc + c_far).reshape(rows_here)

    def apply_month(state, j):
        sb = state.reshape(batch, blk_count, blk_size)
        out = jnp.take(sb, send_idx[:, j], axis=1).transpose(1, 0, 2)
        if j == last_m:
            part = jnp.sum(state * c_all[None, :], axis=1)
            row = jnp.zeros((devices, 8, blk_size), jnp.float32).at[:, 0, :batch].set(part[None, :])
            full = exchange(jnp.concatenate([out, row], axis=1), "grid")
            inventory = jnp.sum(full[:, batch, :batch], axis=0)
            got = full[:, :batch].transpose(1, 0, 2)
        else:
            inventory = None
            got = exchange(out, "grid").transpose(1, 0, 2)
        loc = jnp.take(sb, src_blk[j, :, :near].reshape(-1), axis=1).reshape(batch, blk_count, near, blk_size)
        far = jnp.take(got, src_dev[j, :, near:].reshape(-1), axis=1).reshape(batch, blk_count, FAR, blk_size)
        mixed = jnp.einsum(
            "tbkc,bkrc->tbr",
            loc,
            blocks[j, :, :near],
            precision=PRECISION,
            preferred_element_type=jnp.float32,
        ) + jnp.einsum(
            "tbkc,bkrc->tbr",
            far,
            blocks[j, :, near:],
            precision=PRECISION,
            preferred_element_type=jnp.float32,
        )
        return retain[j][None, :] * state + mixed.reshape(batch, rows_here), inventory

    held = jnp.zeros((batch, rows_here), jnp.float32)
    result = jnp.zeros((own, rows_here), jnp.float32)
    last = sections - 1
    steps = NBATCH + sections - 1
    for step in range(steps):
        if step < NBATCH:
            held = jnp.where(section == 0, tracers[step * batch : (step + 1) * batch], held)
        for j in range(months_here):
            held, inventory = apply_month(held, j)
        b = step - last
        if b >= 0:
            scaled = held * (targets[b * batch : (b + 1) * batch] * points / inventory)[:, None]
            for q in range(batch // own):
                owner = (b * batch + q * own) // own
                piece = scaled[q * own : (q + 1) * own]
                if owner != last:
                    piece = lax.ppermute(piece, "month", [(last, owner)])
                result = jnp.where(section == owner, piece, result)
        if step < steps - 1:
            held = lax.ppermute(held, "month", [(i, (i + 1) % sections) for i in range(sections)])
    return result


def solution(mesh):
    return jax.shard_map(
        local,
        mesh=mesh,
        in_specs=(
            P(None, "grid"),
            P(),
            P("month", "grid"),
            P("month", "grid", None, None, None),
            P("month", "grid", None),
        ),
        out_specs=P("month", "grid"),
        check_vma=False,
    )
```

```python
import jax
import jax.numpy as jnp
from jax import lax
from jax.sharding import PartitionSpec as P

NBATCH = 2
PRECISION = lax.Precision.HIGH
FAR = 2


def exchange(x, axis):
    return lax.all_to_all(x, axis, 0, 0, tiled=True)


def local(tracers, targets, retain, blocks, cols):
    sections = lax.axis_size("month")
    devices = lax.axis_size("grid")
    section = lax.axis_index("month")
    months_here = blocks.shape[0]
    blk_count = blocks.shape[1]
    nk = blocks.shape[2]
    blk_size = blocks.shape[3]
    rows_here = blk_count * blk_size
    points = rows_here * devices
    tracer_count = tracers.shape[0]
    batch = tracer_count // NBATCH
    own = tracer_count // sections

    src_dev = cols // blk_count
    src_blk = cols % blk_count
    near = nk - FAR
    far_dev = src_dev[:, :, near:].reshape(months_here, -1)
    far_blk = src_blk[:, :, near:].reshape(months_here, -1)
    hit = far_dev[:, None, :] == jnp.arange(devices, dtype=jnp.int32)[None, :, None]
    req = jnp.sum(jnp.where(hit, far_blk[:, None, :] + 1, 0), axis=2) - 1

    last_m = months_here - 1
    colsum = jnp.sum(blocks[last_m], axis=2)
    to_blk = src_blk[last_m, :, :near][:, :, None] == jnp.arange(blk_count, dtype=jnp.int32)[None, None, :]
    c_loc = jnp.sum(jnp.where(to_blk[:, :, :, None], colsum[:, :near, None, :], 0.0), axis=(0, 1))
    far_cs = colsum[:, near:].reshape(-1, blk_size)
    cs_send = jnp.sum(jnp.where(hit[last_m][:, :, None], far_cs[None], 0.0), axis=1)
    want = exchange(req.T, "grid")
    send_idx = jnp.maximum(want, 0)
    from_e = want[:, last_m][:, None] == jnp.arange(blk_count, dtype=jnp.int32)[None, :]
    base_c = retain[last_m].reshape(blk_count, blk_size) + c_loc

    def apply_month(state, j, c_all):
        sb = state.reshape(batch, blk_count, blk_size)
        out = jnp.take(sb, send_idx[:, j], axis=1, mode="clip").transpose(1, 0, 2)
        if j == last_m:
            part = jnp.sum(state * c_all[None, :], axis=1)
            row = jnp.zeros((devices, 8, blk_size), jnp.float32).at[:, 0, :batch].set(part[None, :])
            row = row.at[:, 1, :].set(cs_send)
            full = exchange(jnp.concatenate([out, row], axis=1), "grid")
            inventory = jnp.sum(full[:, batch, :batch], axis=0)
            got = full[:, :batch].transpose(1, 0, 2)
            c_far = jnp.sum(jnp.where(from_e[:, :, None], full[:, None, batch + 1, :], 0.0), axis=0)
            c_all = (base_c + c_far).reshape(rows_here)
        else:
            inventory = None
            got = exchange(out, "grid")
            got = got.transpose(1, 0, 2)
        loc = jnp.take(sb, src_blk[j, :, :near].reshape(-1), axis=1, mode="clip").reshape(batch, blk_count, near, blk_size)
        far = jnp.take(got, src_dev[j, :, near:].reshape(-1), axis=1, mode="clip").reshape(batch, blk_count, FAR, blk_size)
        mixed = jnp.einsum(
            "tbkc,bkrc->tbr",
            loc,
            blocks[j, :, :near],
            precision=PRECISION,
            preferred_element_type=jnp.float32,
        ) + jnp.einsum(
            "tbkc,bkrc->tbr",
            far,
            blocks[j, :, near:],
            precision=PRECISION,
            preferred_element_type=jnp.float32,
        )
        return retain[j][None, :] * state + mixed.reshape(batch, rows_here), inventory, c_all

    held = jnp.zeros((batch, rows_here), jnp.float32)
    c_all = jnp.zeros((rows_here,), jnp.float32)
    result = jnp.zeros((own, rows_here), jnp.float32)
    last = sections - 1
    steps = NBATCH + sections - 1
    for step in range(steps):
        if step < NBATCH:
            held = jnp.where(section == 0, tracers[step * batch : (step + 1) * batch], held)
        for j in range(months_here):
            held, inventory, c_all = apply_month(held, j, c_all)
        b = step - last
        if b >= 0:
            scaled = held * (targets[b * batch : (b + 1) * batch] * points / inventory)[:, None]
            for q in range(batch // own):
                owner = (b * batch + q * own) // own
                piece = scaled[q * own : (q + 1) * own]
                if owner != last:
                    piece = lax.ppermute(piece, "month", [(last, owner)])
                result = jnp.where(section == owner, piece, result)
        if step < steps - 1:
            held = lax.ppermute(held, "month", [(i, (i + 1) % sections) for i in range(sections)])
    return result


def solution(mesh):
    return jax.shard_map(
        local,
        mesh=mesh,
        in_specs=(
            P(None, "grid"),
            P(),
            P("month", "grid"),
            P("month", "grid", None, None, None),
            P("month", "grid", None),
        ),
        out_specs=P("month", "grid"),
        check_vma=False,
    )
```

```python
import jax
import jax.numpy as jnp
from jax import lax
from jax.sharding import PartitionSpec as P

NBATCH = 2
PRECISION = lax.Precision.HIGH
FAR = 2


def exchange(x, axis):
    return lax.all_to_all(x, axis, 0, 0, tiled=True)


def local(tracers, targets, retain, blocks, cols):
    sections = lax.axis_size("month")
    devices = lax.axis_size("grid")
    section = lax.axis_index("month")
    months_here = blocks.shape[0]
    blk_count = blocks.shape[1]
    nk = blocks.shape[2]
    blk_size = blocks.shape[3]
    rows_here = blk_count * blk_size
    points = rows_here * devices
    tracer_count = tracers.shape[0]
    batch = tracer_count // NBATCH
    own = tracer_count // sections

    src_dev = cols // blk_count
    src_blk = cols % blk_count
    near = nk - FAR
    far_dev = src_dev[:, :, near:].reshape(months_here, -1)
    far_blk = src_blk[:, :, near:].reshape(months_here, -1)
    hit = far_dev[:, None, :] == jnp.arange(devices, dtype=jnp.int32)[None, :, None]
    req = jnp.sum(jnp.where(hit, far_blk[:, None, :] + 1, 0), axis=2) - 1

    last_m = months_here - 1
    colsum = jnp.sum(blocks[last_m], axis=2)
    to_blk = src_blk[last_m, :, :near][:, :, None] == jnp.arange(blk_count, dtype=jnp.int32)[None, None, :]
    c_loc = jnp.sum(jnp.where(to_blk[:, :, :, None], colsum[:, :near, None, :], 0.0), axis=(0, 1))
    far_cs = colsum[:, near:].reshape(-1, blk_size)
    cs_send = jnp.sum(jnp.where(hit[last_m][:, :, None], far_cs[None], 0.0), axis=1)
    want = exchange(req.T, "grid")
    send_idx = jnp.maximum(want, 0)
    from_e = want[:, last_m][:, None] == jnp.arange(blk_count, dtype=jnp.int32)[None, :]
    base_c = retain[last_m].reshape(blk_count, blk_size) + c_loc

    def apply_month(state, j, c_all, extra):
        sb = state.reshape(batch, blk_count, blk_size)
        out = jnp.take(sb, send_idx[:, j], axis=1, mode="clip").transpose(1, 0, 2)
        if j == last_m and extra:
            part = jnp.sum(state * c_all[None, :], axis=1)
            row = jnp.zeros((devices, 8, blk_size), jnp.float32).at[:, 0, :batch].set(part[None, :])
            row = row.at[:, 1, :].set(cs_send)
            full = exchange(jnp.concatenate([out, row], axis=1), "grid")
            inventory = jnp.sum(full[:, batch, :batch], axis=0)
            got = full[:, :batch].transpose(1, 0, 2)
            c_far = jnp.sum(jnp.where(from_e[:, :, None], full[:, None, batch + 1, :], 0.0), axis=0)
            c_all = (base_c + c_far).reshape(rows_here)
        else:
            inventory = None
            got = exchange(out, "grid")
            got = got.transpose(1, 0, 2)
        loc = jnp.take(sb, src_blk[j, :, :near].reshape(-1), axis=1, mode="clip").reshape(batch, blk_count, near, blk_size)
        far = jnp.take(got, src_dev[j, :, near:].reshape(-1), axis=1, mode="clip").reshape(batch, blk_count, FAR, blk_size)
        mixed = jnp.einsum(
            "tbkc,bkrc->tbr",
            loc,
            blocks[j, :, :near],
            precision=PRECISION,
            preferred_element_type=jnp.float32,
        ) + jnp.einsum(
            "tbkc,bkrc->tbr",
            far,
            blocks[j, :, near:],
            precision=PRECISION,
            preferred_element_type=jnp.float32,
        )
        return retain[j][None, :] * state + mixed.reshape(batch, rows_here), inventory, c_all

    held = jnp.zeros((batch, rows_here), jnp.float32)
    c_all = jnp.zeros((rows_here,), jnp.float32)
    result = jnp.zeros((own, rows_here), jnp.float32)
    last = sections - 1
    steps = NBATCH + sections - 1
    for step in range(steps):
        if step < NBATCH:
            held = jnp.where(section == 0, tracers[step * batch : (step + 1) * batch], held)
        for j in range(months_here):
            held, inventory, c_all = apply_month(held, j, c_all, step == 0 or step >= sections - 1)
        b = step - last
        if b >= 0:
            scaled = held * (targets[b * batch : (b + 1) * batch] * points / inventory)[:, None]
            for q in range(batch // own):
                owner = (b * batch + q * own) // own
                piece = scaled[q * own : (q + 1) * own]
                if owner != last:
                    piece = lax.ppermute(piece, "month", [(last, owner)])
                result = jnp.where(section == owner, piece, result)
        if step < steps - 1:
            held = lax.ppermute(held, "month", [(i, (i + 1) % sections) for i in range(sections)])
    return result


def solution(mesh):
    return jax.shard_map(
        local,
        mesh=mesh,
        in_specs=(
            P(None, "grid"),
            P(),
            P("month", "grid"),
            P("month", "grid", None, None, None),
            P("month", "grid", None),
        ),
        out_specs=P("month", "grid"),
        check_vma=False,
    )
```

```python
import jax
import jax.numpy as jnp
from jax import lax
from jax.sharding import PartitionSpec as P

NBATCH = 2
PRECISION = lax.Precision.HIGH
FAR = 2


def exchange(x, axis):
    return lax.all_to_all(x, axis, 0, 0, tiled=True)


def local(tracers, targets, retain, blocks, cols):
    sections = lax.axis_size("month")
    devices = lax.axis_size("grid")
    section = lax.axis_index("month")
    months_here = blocks.shape[0]
    blk_count = blocks.shape[1]
    nk = blocks.shape[2]
    blk_size = blocks.shape[3]
    rows_here = blk_count * blk_size
    points = rows_here * devices
    tracer_count = tracers.shape[0]
    batch = tracer_count // NBATCH
    own = tracer_count // sections

    src_dev = cols // blk_count
    src_blk = cols % blk_count
    near = nk - FAR
    far_dev = src_dev[:, :, near:].reshape(months_here, -1)
    far_blk = src_blk[:, :, near:].reshape(months_here, -1)
    hit = far_dev[:, None, :] == jnp.arange(devices, dtype=jnp.int32)[None, :, None]
    req = jnp.sum(jnp.where(hit, far_blk[:, None, :] + 1, 0), axis=2) - 1

    last_m = months_here - 1
    colsum = jnp.sum(blocks[last_m, :, :near], axis=2)
    to_blk = src_blk[last_m, :, :near][:, :, None] == jnp.arange(blk_count, dtype=jnp.int32)[None, None, :]
    c_loc = jnp.sum(jnp.where(to_blk[:, :, :, None], colsum[:, :, None, :], 0.0), axis=(0, 1))
    far_cs = jnp.sum(blocks[last_m, :, near:], axis=2).reshape(-1, blk_size)
    cs_send = jnp.sum(jnp.where(hit[last_m][:, :, None], far_cs[None], 0.0), axis=1)
    recv = exchange(jnp.concatenate([cs_send, req.T.astype(jnp.float32)], axis=1), "grid")
    want = jnp.round(recv[:, blk_size:]).astype(jnp.int32)
    send_idx = jnp.maximum(want, 0)
    from_e = want[:, last_m][:, None] == jnp.arange(blk_count, dtype=jnp.int32)[None, :]
    c_far = jnp.sum(jnp.where(from_e[:, :, None], recv[:, None, :blk_size], 0.0), axis=0)
    c_all = (retain[last_m].reshape(blk_count, blk_size) + c_loc + c_far).reshape(rows_here)

    def apply_month(state, j, extra):
        sb = state.reshape(batch, blk_count, blk_size)
        out = jnp.take(sb, send_idx[:, j], axis=1, mode="clip").transpose(1, 0, 2)
        if j == last_m and extra:
            part = jnp.sum(state * c_all[None, :], axis=1)
            row = jnp.zeros((devices, 8, blk_size), jnp.float32).at[:, 0, :batch].set(part[None, :])
            full = exchange(jnp.concatenate([out, row], axis=1), "grid")
            inventory = jnp.sum(full[:, batch, :batch], axis=0)
            got = full[:, :batch].transpose(1, 0, 2)
        else:
            inventory = None
            got = exchange(out, "grid")
            got = got.transpose(1, 0, 2)
        loc = jnp.take(sb, src_blk[j, :, :near].reshape(-1), axis=1, mode="clip").reshape(batch, blk_count, near, blk_size)
        far = jnp.take(got, src_dev[j, :, near:].reshape(-1), axis=1, mode="clip").reshape(batch, blk_count, FAR, blk_size)
        mixed = jnp.einsum(
            "tbkc,bkrc->tbr",
            loc,
            blocks[j, :, :near],
            precision=PRECISION,
            preferred_element_type=jnp.float32,
        ) + jnp.einsum(
            "tbkc,bkrc->tbr",
            far,
            blocks[j, :, near:],
            precision=PRECISION,
            preferred_element_type=jnp.float32,
        )
        return retain[j][None, :] * state + mixed.reshape(batch, rows_here), inventory

    held = jnp.zeros((batch, rows_here), jnp.float32)
    result = jnp.zeros((own, rows_here), jnp.float32)
    last = sections - 1
    steps = NBATCH + sections - 1
    for step in range(steps):
        if step < NBATCH:
            held = jnp.where(section == 0, tracers[step * batch : (step + 1) * batch], held)
        for j in range(months_here):
            held, inventory = apply_month(held, j, step >= sections - 1)
        b = step - last
        if b >= 0:
            scaled = held * (targets[b * batch : (b + 1) * batch] * points / inventory)[:, None]
            for q in range(batch // own):
                owner = (b * batch + q * own) // own
                piece = scaled[q * own : (q + 1) * own]
                if owner != last:
                    piece = lax.ppermute(piece, "month", [(last, owner)])
                result = jnp.where(section == owner, piece, result)
        if step < steps - 1:
            held = lax.ppermute(held, "month", [(i, (i + 1) % sections) for i in range(sections)])
    return result


def solution(mesh):
    return jax.shard_map(
        local,
        mesh=mesh,
        in_specs=(
            P(None, "grid"),
            P(),
            P("month", "grid"),
            P("month", "grid", None, None, None),
            P("month", "grid", None),
        ),
        out_specs=P("month", "grid"),
        check_vma=False,
    )
```
